512 devices in a mesh: row: 16 (over y, z_hi), col: 32 (over x, z_lo, core).
Axes of the slice: x: 4, y: 8, z: 8 (z_hi: 2, z_lo: 4; z = z_hi * 4 + z_lo), core: 2. Of those that a mesh axis runs over, the one named last changes fastest.
Arguments:
- points: bfloat16 [81920, 128], P(('row', 'col')), may hold values from -6 to 6
- w_in: bfloat16 [128, 1024], replicated, may hold values from -0.5 to 0.5
- w_mid: bfloat16 [1024, 1024], replicated, may hold values from -0.1875 to 0.1875
- w_out: bfloat16 [1024, 32], replicated, may hold values from -0.1875 to 0.1875
- lengthscale: float32 [32], replicated, may hold values from 1 to 10
- probes: bfloat16 [8, 81920], P(None, ('row', 'col')), may hold values from -0.0546875 to 0.0546875
Outputs:
- kv: float32 [8, 81920], P(None, ('row', 'col'))
The draws below stay inside these ranges and needn't reach their ends.
All inputs are finite; a program needn't handle non-finite values.
Results may differ from the reference program's by a relative error of at most 0.0055.
Values may be sent and summed in bfloat16 or wider, within the bound.
No kernel may reach another device: no remote copies, remote signals or barrier semaphores. Data moves between devices by JAX's collectives and lax.ppermute only.
A program may use at most 64 MiB of HBM per device.

```python
import math
import jax
import jax.numpy as jnp
from jax import lax

IN = 128
HID = 1024
FEAT = 32
PROBES = 8
POINTS = 81920


def block_scale(stream_key, shape, cuts, least, high):
    level = 1.0
    for axis_at, shards_of in cuts:
        heights = jax.random.uniform(jax.random.fold_in(jax.random.fold_in(stream_key, 6), axis_at), (shards_of,), jnp.float32, least / len(cuts), high / len(cuts))
        level = level * jnp.repeat(jnp.exp(heights), shape[axis_at] // shards_of).reshape((-1,) + (1,) * (len(shape) - 1 - axis_at))
    return level


def bell_draw(rng, dims, spread, limit, shards=(), kind=jnp.bfloat16):
    factor_of = block_scale(rng, dims, shards, -0.22, 0.18) if shards else 1.0
    values = jax.random.normal(rng, dims, jnp.float32) * spread * factor_of
    return jnp.minimum(jnp.maximum(values, -limit), limit).astype(kind)


def setup_inputs(seed: int = 0) -> dict:
    arg_keys = jax.random.split(jax.random.key(seed), 7)
    return {
        "points": bell_draw(arg_keys[0], (POINTS, IN), 1.0, 6.0, ((0, 512),)),
        "w_in": bell_draw(arg_keys[1], (IN, HID), IN ** -0.5, 0.5),
        "w_mid": bell_draw(arg_keys[2], (HID, HID), HID ** -0.5, 0.1875),
        "w_out": bell_draw(arg_keys[3], (HID, FEAT), HID ** -0.5, 0.1875),
        "lengthscale": jnp.clip(jnp.exp(jax.random.uniform(arg_keys[4], (FEAT,), jnp.float32, math.log(1.0), math.log(10.0))), 1.0, 10.0),
        "probes": bell_draw(arg_keys[5], (PROBES, POINTS), (POINTS ** -0.5), 0.0546875, ((1, 512),)),
    }


def wide_dot(left, right):
    return jnp.dot(left.astype(jnp.float32), right.astype(jnp.float32), precision=lax.Precision.HIGHEST)

def reference(points, w_in, w_mid, w_out, lengthscale, probes):
    hidden_one = jax.nn.relu(wide_dot(points, w_in)).astype(jnp.bfloat16)
    hidden_two = jax.nn.relu(wide_dot(hidden_one, w_mid)).astype(jnp.bfloat16)
    features = wide_dot(hidden_two, w_out).T
    scaled = (features / lengthscale[:, None]).astype(jnp.bfloat16)
    scaled_wide = scaled.astype(jnp.float32)
    sq_norm = lax.optimization_barrier(jnp.sum(scaled_wide * scaled_wide, axis=0))
    probes_wide = probes.astype(jnp.float32)
    block_rows = math.gcd(POINTS, 512)

    def one_block(block_start):
        left_feats = lax.dynamic_slice_in_dim(scaled_wide, block_start, block_rows, 1)
        left_sq = lax.dynamic_slice_in_dim(sq_norm, block_start, block_rows, 0)
        cross_term = jnp.dot(left_feats.T, scaled_wide, precision=lax.Precision.HIGHEST)
        dist_sq = jnp.maximum(left_sq[:, None] + sq_norm[None, :] - 2.0 * cross_term, 0.0)
        scaled_dist = jnp.sqrt(5.0 * dist_sq)
        kernel = ((1.0 + scaled_dist + scaled_dist * scaled_dist / 3.0) * jnp.exp(-scaled_dist)).astype(jnp.bfloat16)
        return jnp.dot(probes_wide, kernel.astype(jnp.float32).T, precision=lax.Precision.HIGHEST)
    starts = jnp.arange(POINTS // block_rows, dtype=jnp.int32) * block_rows
    blocks = lax.map(one_block, starts)
    return jnp.transpose(blocks, (1, 0, 2)).reshape(probes.shape[0], POINTS)
```

```python
import jax
import jax.numpy as jnp
from jax import lax
from jax.sharding import PartitionSpec as P


def dot_f32(left, right, dims):
    return lax.dot_general(
        left, right, (dims, ((), ())), preferred_element_type=jnp.float32
    )


def matern_tile(left_feats, left_sq, right_feats):
    cross_term = dot_f32(left_feats, right_feats, ((0,), (0,)))
    right_wide = right_feats.astype(jnp.float32)
    right_sq = jnp.sum(right_wide * right_wide, axis=0)
    dist_sq = jnp.maximum(left_sq[:, None] + right_sq[None, :] - 2.0 * cross_term, 0.0)
    scaled_dist = jnp.sqrt(5.0 * dist_sq)
    values = (1.0 + scaled_dist + scaled_dist * scaled_dist / 3.0) * jnp.exp(-scaled_dist)
    return values.astype(jnp.bfloat16)


def gather_peers(block, axis, peers):
    spread = jnp.broadcast_to(block[None], (peers,) + block.shape)
    arrived = lax.all_to_all(spread, axis, 0, 0, tiled=False)
    rows = block.shape[0]
    return jnp.transpose(arrived, (1, 0, 2)).reshape(rows, peers * block.shape[1])


def on_device(points, w_in, w_mid, w_out, lengthscale, probes):
    hidden_one = jax.nn.relu(dot_f32(points, w_in, ((1,), (0,)))).astype(jnp.bfloat16)
    hidden_two = jax.nn.relu(dot_f32(hidden_one, w_mid, ((1,), (0,)))).astype(jnp.bfloat16)
    features = dot_f32(w_out, hidden_two, ((0,), (1,)))
    scaled = (features / lengthscale[:, None]).astype(jnp.bfloat16)
    col_peers = lax.axis_size("col")
    row_peers = lax.axis_size("row")
    local = scaled.shape[1]
    feat_dim = scaled.shape[0]
    probe_rows = probes.shape[0]
    row_feats = gather_peers(scaled, "col", col_peers)
    row_wide = row_feats.astype(jnp.float32)
    row_sq = jnp.sum(row_wide * row_wide, axis=0)
    joined = jnp.concatenate([scaled, probes], axis=0)
    piece = gather_peers(joined, "row", row_peers)
    piece_feats = piece[:feat_dim]
    piece_probes = piece[feat_dim:]
    block_cols = 256
    initial = jnp.zeros((probe_rows, row_feats.shape[1]), jnp.float32)

    def advance(position, row_acc):
        column_start = position * block_cols
        feats_block = lax.dynamic_slice_in_dim(piece_feats, column_start, block_cols, 1)
        probes_block = lax.dynamic_slice_in_dim(piece_probes, column_start, block_cols, 1)
        kernel_tile = matern_tile(row_feats, row_sq, feats_block)
        return row_acc + dot_f32(probes_block, kernel_tile, ((1,), (1,)))

    folded = lax.fori_loop(0, piece_feats.shape[1] // block_cols, advance, initial)
    parts = jnp.transpose(folded.reshape(probe_rows, col_peers, local), (1, 0, 2))
    arrived = lax.all_to_all(parts, "col", 0, 0, tiled=False)
    return jnp.sum(arrived, axis=0)


def solution(mesh):
    in_specs = (P(("row", "col"), None), P(), P(), P(), P(), P(None, ("row", "col")))
    out_specs = P(None, ("row", "col"))
    return jax.shard_map(
        on_device, mesh=mesh, in_specs=in_specs, out_specs=out_specs, check_vma=False
    )
```

```python
import jax
import jax.numpy as jnp
from jax import lax
from jax.sharding import PartitionSpec as P


def dot_f32(left, right, dims):
    return lax.dot_general(
        left, right, (dims, ((), ())), preferred_element_type=jnp.float32
    )


def matern_tile(left_feats, left_sq, right_feats):
    cross_term = dot_f32(left_feats, right_feats, ((0,), (0,)))
    right_wide = right_feats.astype(jnp.float32)
    right_sq = jnp.sum(right_wide * right_wide, axis=0)
    dist_sq = jnp.maximum(left_sq[:, None] + right_sq[None, :] - 2.0 * cross_term, 0.0)
    scaled_dist = jnp.sqrt(5.0 * dist_sq)
    values = (1.0 + scaled_dist + scaled_dist * scaled_dist / 3.0) * jnp.exp(-scaled_dist)
    return values.astype(jnp.bfloat16)


def gather_peers(block, axis, peers):
    spread = jnp.broadcast_to(block[None], (peers,) + block.shape)
    arrived = lax.all_to_all(spread, axis, 0, 0, tiled=False)
    rows = block.shape[0]
    return jnp.transpose(arrived, (1, 0, 2)).reshape(rows, peers * block.shape[1])


def fold_columns(row_feats, row_sq, feats, probes, acc, block_cols):
    def advance(position, row_acc):
        column_start = position * block_cols
        feats_block = lax.dynamic_slice_in_dim(feats, column_start, block_cols, 1)
        probes_block = lax.dynamic_slice_in_dim(probes, column_start, block_cols, 1)
        kernel_tile = matern_tile(row_feats, row_sq, feats_block)
        return row_acc + dot_f32(probes_block, kernel_tile, ((1,), (1,)))

    return lax.fori_loop(0, feats.shape[1] // block_cols, advance, acc)


def on_device(points, w_in, w_mid, w_out, lengthscale, probes):
    hidden_one = jax.nn.relu(dot_f32(points, w_in, ((1,), (0,)))).astype(jnp.bfloat16)
    hidden_two = jax.nn.relu(dot_f32(hidden_one, w_mid, ((1,), (0,)))).astype(jnp.bfloat16)
    features = dot_f32(w_out, hidden_two, ((0,), (1,)))
    scaled = (features / lengthscale[:, None]).astype(jnp.bfloat16)
    col_peers = lax.axis_size("col")
    row_peers = lax.axis_size("row")
    local = scaled.shape[1]
    feat_dim = scaled.shape[0]
    probe_rows = probes.shape[0]
    joined = jnp.concatenate([scaled, probes], axis=0)
    block = gather_peers(joined, "col", col_peers)
    row_feats = block[:feat_dim]
    row_wide = row_feats.astype(jnp.float32)
    row_sq = jnp.sum(row_wide * row_wide, axis=0)
    halves = col_peers // row_peers
    span = block.shape[1] // halves
    col = lax.axis_index("col")
    mine = lax.dynamic_slice_in_dim(block, (col % halves) * span, span, 1)
    pairs = []
    for r in range(row_peers):
        for c in range(col_peers):
            target = (r - c // halves) % row_peers
            pairs.append((r * col_peers + c, target * col_peers + c))
    chunks = 2
    width = span // chunks
    arrived = [
        lax.ppermute(mine[:, k * width:(k + 1) * width], ("row", "col"), pairs)
        for k in range(chunks)
    ]
    acc = jnp.zeros((probe_rows, block.shape[1]), jnp.float32)
    for piece in arrived:
        acc = fold_columns(row_feats, row_sq, piece[:feat_dim], piece[feat_dim:], acc, 256)
    parts = jnp.transpose(acc.reshape(probe_rows, col_peers, local), (1, 0, 2))
    summed = lax.all_to_all(parts, "col", 0, 0, tiled=False)
    return jnp.sum(summed, axis=0)


def solution(mesh):
    in_specs = (P(("row", "col"), None), P(), P(), P(), P(), P(None, ("row", "col")))
    out_specs = P(None, ("row", "col"))
    return jax.shard_map(
        on_device, mesh=mesh, in_specs=in_specs, out_specs=out_specs, check_vma=False
    )
```

```python
import jax
import jax.numpy as jnp
from jax import lax
from jax.sharding import PartitionSpec as P


def dot_f32(left, right, dims):
    return lax.dot_general(
        left, right, (dims, ((), ())), preferred_element_type=jnp.float32
    )


def split_three(value):
    high = value.astype(jnp.bfloat16)
    rest = value - high.astype(jnp.float32)
    middle = rest.astype(jnp.bfloat16)
    low = (rest - middle.astype(jnp.float32)).astype(jnp.bfloat16)
    return [high, middle, low]


def row_side(feats):
    wide = feats.astype(jnp.float32)
    five_sq = 5.0 * jnp.sum(wide * wide, axis=0)
    ones = jnp.ones((3, feats.shape[1]), jnp.bfloat16)
    return jnp.concatenate([jnp.stack(split_three(five_sq)), ones, feats, feats], axis=0)


def column_side(feats):
    wide = feats.astype(jnp.float32)
    five_sq = 5.0 * jnp.sum(wide * wide, axis=0)
    ones = jnp.ones((3, feats.shape[1]), jnp.bfloat16)
    scaled = -10.0 * wide
    high = scaled.astype(jnp.bfloat16)
    low = (scaled - high.astype(jnp.float32)).astype(jnp.bfloat16)
    return jnp.concatenate([ones, jnp.stack(split_three(five_sq)), high, low], axis=0)


def matern_tile(left_side, right_side):
    five_dist = jnp.maximum(dot_f32(left_side, right_side, ((0,), (0,))), 0.0)
    scaled_dist = jnp.sqrt(five_dist)
    values = (1.0 + scaled_dist + five_dist * (1.0 / 3.0)) * jnp.exp(-scaled_dist)
    return values.astype(jnp.bfloat16)


def gather_peers(block, axis, peers):
    spread = jnp.broadcast_to(block[None], (peers,) + block.shape)
    arrived = lax.all_to_all(spread, axis, 0, 0, tiled=False)
    rows = block.shape[0]
    return jnp.transpose(arrived, (1, 0, 2)).reshape(rows, peers * block.shape[1])


def fold_columns(left_side, right_side, probes, acc, block_cols):
    def advance(position, row_acc):
        column_start = position * block_cols
        side_block = lax.dynamic_slice_in_dim(right_side, column_start, block_cols, 1)
        probes_block = lax.dynamic_slice_in_dim(probes, column_start, block_cols, 1)
        kernel_tile = matern_tile(left_side, side_block)
        return row_acc + dot_f32(probes_block, kernel_tile, ((1,), (1,)))

    return lax.fori_loop(0, right_side.shape[1] // block_cols, advance, acc)


def on_device(points, w_in, w_mid, w_out, lengthscale, probes):
    hidden_one = jax.nn.relu(dot_f32(points, w_in, ((1,), (0,)))).astype(jnp.bfloat16)
    hidden_two = jax.nn.relu(dot_f32(hidden_one, w_mid, ((1,), (0,)))).astype(jnp.bfloat16)
    features = dot_f32(w_out, hidden_two, ((0,), (1,)))
    scaled = (features / lengthscale[:, None]).astype(jnp.bfloat16)
    col_peers = lax.axis_size("col")
    row_peers = lax.axis_size("row")
    local = scaled.shape[1]
    feat_dim = scaled.shape[0]
    probe_rows = probes.shape[0]
    joined = jnp.concatenate([scaled, probes], axis=0)
    block = gather_peers(joined, "col", col_peers)
    left_side = row_side(block[:feat_dim])
    halves = col_peers // row_peers
    span = block.shape[1] // halves
    col = lax.axis_index("col")
    mine = lax.dynamic_slice_in_dim(block, (col % halves) * span, span, 1)
    pairs = []
    for r in range(row_peers):
        for c in range(col_peers):
            target = (r - c // halves) % row_peers
            pairs.append((r * col_peers + c, target * col_peers + c))
    chunks = 2
    width = span // chunks
    arrived = [
        lax.ppermute(mine[:, k * width:(k + 1) * width], ("row", "col"), pairs)
        for k in range(chunks)
    ]
    acc = jnp.zeros((probe_rows, block.shape[1]), jnp.float32)
    for piece in arrived:
        right_side = column_side(piece[:feat_dim])
        acc = fold_columns(left_side, right_side, piece[feat_dim:], acc, 256)
    parts = jnp.transpose(acc.reshape(probe_rows, col_peers, local), (1, 0, 2))
    summed = lax.all_to_all(parts, "col", 0, 0, tiled=False)
    return jnp.sum(summed, axis=0)


def solution(mesh):
    in_specs = (P(("row", "col"), None), P(), P(), P(), P(), P(None, ("row", "col")))
    out_specs = P(None, ("row", "col"))
    return jax.shard_map(
        on_device, mesh=mesh, in_specs=in_specs, out_specs=out_specs, check_vma=False
    )
```

```python
import jax
import jax.numpy as jnp
from jax import lax
from jax.sharding import PartitionSpec as P


def dot_f32(left, right, dims):
    return lax.dot_general(
        left, right, (dims, ((), ())), preferred_element_type=jnp.float32
    )


def five_sq_norm(feats):
    wide = feats.astype(jnp.float32)
    return 5.0 * jnp.sum(wide * wide, axis=0)


def minus_ten(feats):
    scaled = -10.0 * feats.astype(jnp.float32)
    high = lax.reduce_precision(scaled, exponent_bits=8, mantissa_bits=7)
    low = scaled - high
    return jnp.concatenate([high.astype(jnp.bfloat16), low.astype(jnp.bfloat16)], axis=0)


def matern_tile(left_feats, left_sq5, right_side, right_sq5):
    cross_term = dot_f32(left_feats, right_side, ((0,), (0,)))
    five_dist = jnp.maximum(left_sq5[:, None] + right_sq5[None, :] + cross_term, 0.0)
    scaled_dist = jnp.sqrt(five_dist)
    values = (1.0 + scaled_dist + five_dist * (1.0 / 3.0)) * jnp.exp(-scaled_dist)
    return values.astype(jnp.bfloat16)


def gather_peers(block, axis, peers):
    spread = jnp.broadcast_to(block[None], (peers,) + block.shape)
    arrived = lax.all_to_all(spread, axis, 0, 0, tiled=False)
    rows = block.shape[0]
    return jnp.transpose(arrived, (1, 0, 2)).reshape(rows, peers * block.shape[1])


def fold_columns(left_feats, left_sq5, right_side, right_sq5, probes, acc, block_cols):
    doubled = jnp.concatenate([left_feats, left_feats], axis=0)

    def advance(position, row_acc):
        column_start = position * block_cols
        side_block = lax.dynamic_slice_in_dim(right_side, column_start, block_cols, 1)
        sq_block = lax.dynamic_slice_in_dim(right_sq5, column_start, block_cols, 0)
        probes_block = lax.dynamic_slice_in_dim(probes, column_start, block_cols, 1)
        kernel_tile = matern_tile(doubled, left_sq5, side_block, sq_block)
        return row_acc + dot_f32(probes_block, kernel_tile, ((1,), (1,)))

    return lax.fori_loop(0, right_side.shape[1] // block_cols, advance, acc)


def on_device(points, w_in, w_mid, w_out, lengthscale, probes):
    hidden_one = jax.nn.relu(dot_f32(points, w_in, ((1,), (0,)))).astype(jnp.bfloat16)
    hidden_two = jax.nn.relu(dot_f32(hidden_one, w_mid, ((1,), (0,)))).astype(jnp.bfloat16)
    features = dot_f32(w_out, hidden_two, ((0,), (1,)))
    scaled = (features / lengthscale[:, None]).astype(jnp.bfloat16)
    col_peers = lax.axis_size("col")
    row_peers = lax.axis_size("row")
    local = scaled.shape[1]
    feat_dim = scaled.shape[0]
    probe_rows = probes.shape[0]
    joined = jnp.concatenate([scaled, probes], axis=0)
    block = gather_peers(joined, "col", col_peers)
    row_feats = block[:feat_dim]
    row_sq5 = five_sq_norm(row_feats)
    halves = col_peers // row_peers
    span = block.shape[1] // halves
    col = lax.axis_index("col")
    mine = lax.dynamic_slice_in_dim(block, (col % halves) * span, span, 1)
    pairs = []
    for r in range(row_peers):
        for c in range(col_peers):
            target = (r - c // halves) % row_peers
            pairs.append((r * col_peers + c, target * col_peers + c))
    chunks = 1
    width = span // chunks
    arrived = [
        lax.ppermute(mine[:, k * width:(k + 1) * width], ("row", "col"), pairs)
        for k in range(chunks)
    ]
    acc = jnp.zeros((probe_rows, block.shape[1]), jnp.float32)
    for piece in arrived:
        col_feats = piece[:feat_dim]
        acc = fold_columns(
            row_feats, row_sq5, minus_ten(col_feats), five_sq_norm(col_feats),
            piece[feat_dim:], acc, 256,
        )
    parts = jnp.transpose(acc.reshape(probe_rows, col_peers, local), (1, 0, 2))
    summed = lax.all_to_all(parts, "col", 0, 0, tiled=False)
    return jnp.sum(summed, axis=0)


def solution(mesh):
    in_specs = (P(("row", "col"), None), P(), P(), P(), P(), P(None, ("row", "col")))
    out_specs = P(None, ("row", "col"))
    return jax.shard_map(
        on_device, mesh=mesh, in_specs=in_specs, out_specs=out_specs, check_vma=False
    )
```

```python
import functools

import jax
import jax.numpy as jnp
from jax import lax
from jax.experimental import pallas as pl
from jax.sharding import PartitionSpec as P


def dot_f32(left, right, dims):
    return lax.dot_general(
        left, right, (dims, ((), ())), preferred_element_type=jnp.float32
    )


def five_sq_norm(feats):
    wide = feats.astype(jnp.float32)
    return 5.0 * jnp.sum(wide * wide, axis=0)


def minus_ten(feats):
    scaled = -10.0 * feats.astype(jnp.float32)
    high = lax.reduce_precision(scaled, exponent_bits=8, mantissa_bits=7)
    low = scaled - high
    return jnp.concatenate([high.astype(jnp.bfloat16), low.astype(jnp.bfloat16)], axis=0)


def matern_kernel(lhs_ref, lsq_ref, rhs_ref, rsq_ref, pr_ref, out_ref, *, sub):
    @pl.when(pl.program_id(1) == 0)
    def _():
        out_ref[...] = jnp.zeros_like(out_ref)

    rhs = rhs_ref[...]
    rsq = rsq_ref[...]
    probes = pr_ref[...]

    def body(step, carry):
        start = pl.multiple_of(step * sub, sub)
        cross = jnp.dot(lhs_ref[pl.ds(start, sub), :], rhs, preferred_element_type=jnp.float32)
        five_dist = jnp.maximum(lsq_ref[pl.ds(start, sub), :] + rsq + cross, 0.0)
        scaled_dist = jnp.sqrt(five_dist)
        values = (1.0 + scaled_dist + five_dist * (1.0 / 3.0)) * jnp.exp(-scaled_dist)
        tile = values.astype(jnp.bfloat16)
        part = lax.dot_general(probes, tile, (((1,), (1,)), ((), ())), preferred_element_type=jnp.float32)
        out_ref[:, pl.ds(start, sub)] += part
        return carry

    lax.fori_loop(0, lhs_ref.shape[0] // sub, body, 0)


def matern_probes(lhs, lsq, rhs, rsq, probes, rows_tile=640, cols_tile=1280, sub=128):
    rows = lhs.shape[0]
    cols = rhs.shape[1]
    depth = lhs.shape[1]
    grid = (rows // rows_tile, cols // cols_tile)
    return pl.pallas_call(
        functools.partial(matern_kernel, sub=sub),
        out_shape=jax.ShapeDtypeStruct((probes.shape[0], rows), jnp.float32),
        grid=grid,
        in_specs=[
            pl.BlockSpec((rows_tile, depth), lambda i, j: (i, 0)),
            pl.BlockSpec((rows_tile, 1), lambda i, j: (i, 0)),
            pl.BlockSpec((depth, cols_tile), lambda i, j: (0, j)),
            pl.BlockSpec((1, cols_tile), lambda i, j: (0, j)),
            pl.BlockSpec((probes.shape[0], cols_tile), lambda i, j: (0, j)),
        ],
        out_specs=pl.BlockSpec((probes.shape[0], rows_tile), lambda i, j: (0, i)),
        cost_estimate=pl.CostEstimate(
            flops=2 * rows * cols * (depth + probes.shape[0]) + 12 * rows * cols,
            transcendentals=2 * rows * cols,
            bytes_accessed=2 * (rows * depth + cols * depth) + 4 * rows * 8,
        ),
    )(lhs, lsq, rhs, rsq, probes)


def gather_peers(block, axis, peers):
    spread = jnp.broadcast_to(block[None], (peers,) + block.shape)
    arrived = lax.all_to_all(spread, axis, 0, 0, tiled=False)
    rows = block.shape[0]
    return jnp.transpose(arrived, (1, 0, 2)).reshape(rows, peers * block.shape[1])


def on_device(points, w_in, w_mid, w_out, lengthscale, probes):
    hidden_one = jax.nn.relu(dot_f32(points, w_in, ((1,), (0,)))).astype(jnp.bfloat16)
    hidden_two = jax.nn.relu(dot_f32(hidden_one, w_mid, ((1,), (0,)))).astype(jnp.bfloat16)
    features = dot_f32(w_out, hidden_two, ((0,), (1,)))
    scaled = (features / lengthscale[:, None]).astype(jnp.bfloat16)
    col_peers = lax.axis_size("col")
    row_peers = lax.axis_size("row")
    local = scaled.shape[1]
    feat_dim = scaled.shape[0]
    probe_rows = probes.shape[0]
    joined = jnp.concatenate([scaled, probes], axis=0)
    block = gather_peers(joined, "col", col_peers)
    row_feats = block[:feat_dim]
    row_sq5 = five_sq_norm(row_feats)
    halves = col_peers // row_peers
    span = block.shape[1] // halves
    col = lax.axis_index("col")
    mine = lax.dynamic_slice_in_dim(block, (col % halves) * span, span, 1)
    pairs = []
    for r in range(row_peers):
        for c in range(col_peers):
            target = (r - c // halves) % row_peers
            pairs.append((r * col_peers + c, target * col_peers + c))
    chunks = 1
    width = span // chunks
    arrived = [
        lax.ppermute(mine[:, k * width:(k + 1) * width], ("row", "col"), pairs)
        for k in range(chunks)
    ]
    (piece,) = arrived
    col_feats = piece[:feat_dim]
    lhs = jnp.concatenate([row_feats, row_feats], axis=0).T
    acc = matern_probes(
        lhs, row_sq5[:, None], minus_ten(col_feats), five_sq_norm(col_feats)[None, :],
        piece[feat_dim:],
    )
    parts = jnp.transpose(acc.reshape(probe_rows, col_peers, local), (1, 0, 2))
    summed = lax.all_to_all(parts, "col", 0, 0, tiled=False)
    return jnp.sum(summed, axis=0)


def solution(mesh):
    in_specs = (P(("row", "col"), None), P(), P(), P(), P(), P(None, ("row", "col")))
    out_specs = P(None, ("row", "col"))
    return jax.shard_map(
        on_device, mesh=mesh, in_specs=in_specs, out_specs=out_specs, check_vma=False
    )
```

```python
import functools

import jax
import jax.numpy as jnp
from jax import lax
from jax.experimental import pallas as pl
from jax.sharding import PartitionSpec as P


def dot_f32(left, right, dims):
    return lax.dot_general(
        left, right, (dims, ((), ())), preferred_element_type=jnp.float32
    )


def five_sq_norm(feats):
    wide = feats.astype(jnp.float32)
    return 5.0 * jnp.sum(wide * wide, axis=0)


def minus_ten(feats):
    scaled = -10.0 * feats.astype(jnp.float32)
    high = lax.reduce_precision(scaled, exponent_bits=8, mantissa_bits=7)
    low = scaled - high
    return jnp.concatenate([high.astype(jnp.bfloat16), low.astype(jnp.bfloat16)], axis=0)


def matern_kernel(lhs_ref, lsq_ref, rhs_ref, rsq_ref, prt_ref, out_ref, *, rows_sub, cols_sub):
    @pl.when(pl.program_id(1) == 0)
    def _():
        out_ref[...] = jnp.zeros_like(out_ref)

    def col_body(col_step, carry):
        col_start = pl.multiple_of(col_step * cols_sub, cols_sub)
        rhs = rhs_ref[:, pl.ds(col_start, cols_sub)]
        rsq = rsq_ref[:, pl.ds(col_start, cols_sub)]
        probes_t = prt_ref[pl.ds(col_start, cols_sub), :]

        def row_body(row_step, inner):
            row_start = pl.multiple_of(row_step * rows_sub, rows_sub)
            cross = jnp.dot(
                lhs_ref[pl.ds(row_start, rows_sub), :], rhs,
                preferred_element_type=jnp.float32,
            )
            five_dist = jnp.maximum(lsq_ref[pl.ds(row_start, rows_sub), :] + rsq + cross, 0.0)
            scaled_dist = jnp.sqrt(five_dist)
            values = (1.0 + scaled_dist + five_dist * (1.0 / 3.0)) * jnp.exp(-scaled_dist)
            tile = values.astype(jnp.bfloat16)
            out_ref[pl.ds(row_start, rows_sub), :] += jnp.dot(
                tile, probes_t, preferred_element_type=jnp.float32
            )
            return inner

        lax.fori_loop(0, lhs_ref.shape[0] // rows_sub, row_body, 0)
        return carry

    lax.fori_loop(0, rhs_ref.shape[1] // cols_sub, col_body, 0)


def matern_probes(lhs, lsq, rhs, rsq, probes_t, rows_tile=1280, cols_tile=1280,
                  rows_sub=128, cols_sub=256):
    rows = lhs.shape[0]
    cols = rhs.shape[1]
    depth = lhs.shape[1]
    probe_rows = probes_t.shape[1]
    grid = (rows // rows_tile, cols // cols_tile)
    return pl.pallas_call(
        functools.partial(matern_kernel, rows_sub=rows_sub, cols_sub=cols_sub),
        out_shape=jax.ShapeDtypeStruct((rows, probe_rows), jnp.float32),
        grid=grid,
        in_specs=[
            pl.BlockSpec((rows_tile, depth), lambda i, j: (i, 0)),
            pl.BlockSpec((rows_tile, 1), lambda i, j: (i, 0)),
            pl.BlockSpec((depth, cols_tile), lambda i, j: (0, j)),
            pl.BlockSpec((1, cols_tile), lambda i, j: (0, j)),
            pl.BlockSpec((cols_tile, probe_rows), lambda i, j: (j, 0)),
        ],
        out_specs=pl.BlockSpec((rows_tile, probe_rows), lambda i, j: (i, 0)),
        cost_estimate=pl.CostEstimate(
            flops=2 * rows * cols * (depth + probe_rows) + 12 * rows * cols,
            transcendentals=2 * rows * cols,
            bytes_accessed=2 * (rows * depth + cols * depth) + 4 * rows * probe_rows,
        ),
    )(lhs, lsq, rhs, rsq, probes_t)


def gather_peers(block, axis, peers):
    spread = jnp.broadcast_to(block[None], (peers,) + block.shape)
    arrived = lax.all_to_all(spread, axis, 0, 0, tiled=False)
    rows = block.shape[0]
    return jnp.transpose(arrived, (1, 0, 2)).reshape(rows, peers * block.shape[1])


def on_device(points, w_in, w_mid, w_out, lengthscale, probes):
    hidden_one = jax.nn.relu(dot_f32(points, w_in, ((1,), (0,)))).astype(jnp.bfloat16)
    hidden_two = jax.nn.relu(dot_f32(hidden_one, w_mid, ((1,), (0,)))).astype(jnp.bfloat16)
    features = dot_f32(w_out, hidden_two, ((0,), (1,)))
    scaled = (features / lengthscale[:, None]).astype(jnp.bfloat16)
    col_peers = lax.axis_size("col")
    row_peers = lax.axis_size("row")
    local = scaled.shape[1]
    feat_dim = scaled.shape[0]
    probe_rows = probes.shape[0]
    joined = jnp.concatenate([scaled, probes], axis=0)
    block = gather_peers(joined, "col", col_peers)
    row_feats = block[:feat_dim]
    row_sq5 = five_sq_norm(row_feats)
    halves = col_peers // row_peers
    span = block.shape[1] // halves
    col = lax.axis_index("col")
    mine = lax.dynamic_slice_in_dim(block, (col % halves) * span, span, 1)
    pairs = []
    for r in range(row_peers):
        for c in range(col_peers):
            target = (r - c // halves) % row_peers
            pairs.append((r * col_peers + c, target * col_peers + c))
    chunks = 1
    width = span // chunks
    arrived = [
        lax.ppermute(mine[:, k * width:(k + 1) * width], ("row", "col"), pairs)
        for k in range(chunks)
    ]
    (piece,) = arrived
    col_feats = piece[:feat_dim]
    lhs = jnp.concatenate([row_feats, row_feats], axis=0).T
    acc = matern_probes(
        lhs, row_sq5[:, None], minus_ten(col_feats), five_sq_norm(col_feats)[None, :],
        piece[feat_dim:].T,
    )
    parts = jnp.transpose(acc.reshape(col_peers, local, probe_rows), (0, 2, 1))
    summed = lax.all_to_all(parts, "col", 0, 0, tiled=False)
    return jnp.sum(summed, axis=0)


def solution(mesh):
    in_specs = (P(("row", "col"), None), P(), P(), P(), P(), P(None, ("row", "col")))
    out_specs = P(None, ("row", "col"))
    return jax.shard_map(
        on_device, mesh=mesh, in_specs=in_specs, out_specs=out_specs, check_vma=False
    )
```

```python
import jax
import jax.numpy as jnp
from jax import lax
from jax.sharding import PartitionSpec as P


def dot_f32(left, right, dims):
    return lax.dot_general(
        left, right, (dims, ((), ())), preferred_element_type=jnp.float32
    )


def split_three(value):
    high = lax.reduce_precision(value, exponent_bits=8, mantissa_bits=7)
    rest = value - high
    middle = lax.reduce_precision(rest, exponent_bits=8, mantissa_bits=7)
    low = rest - middle
    return jnp.stack([high, middle, low]).astype(jnp.bfloat16)


def augmented(feats):
    wide = feats.astype(jnp.float32)
    sq_norm = jnp.sum(wide * wide, axis=0)
    ones = jnp.ones((3, feats.shape[1]), jnp.bfloat16)
    return jnp.concatenate([feats, split_three(sq_norm), ones], axis=0)


def column_side(side, feat_dim):
    doubled = (side[:feat_dim].astype(jnp.float32) * -2.0).astype(jnp.bfloat16)
    return jnp.concatenate(
        [doubled, side[feat_dim + 3:feat_dim + 6], side[feat_dim:feat_dim + 3]], axis=0
    )


def matern_tile(left_side, right_side):
    dist_sq = jnp.maximum(dot_f32(left_side, right_side, ((0,), (0,))), 0.0)
    scaled_dist = jnp.sqrt(5.0 * dist_sq)
    values = (1.0 + scaled_dist + scaled_dist * scaled_dist / 3.0) * jnp.exp(-scaled_dist)
    return values.astype(jnp.bfloat16)


def gather_peers(block, axis, peers):
    spread = jnp.broadcast_to(block[None], (peers,) + block.shape)
    arrived = lax.all_to_all(spread, axis, 0, 0, tiled=False)
    rows = block.shape[0]
    return jnp.transpose(arrived, (1, 0, 2)).reshape(rows, peers * block.shape[1])


def fold_columns(left_side, right_side, probes, acc, block_cols):
    def advance(position, row_acc):
        column_start = position * block_cols
        side_block = lax.dynamic_slice_in_dim(right_side, column_start, block_cols, 1)
        probes_block = lax.dynamic_slice_in_dim(probes, column_start, block_cols, 1)
        kernel_tile = matern_tile(left_side, side_block)
        return row_acc + dot_f32(probes_block, kernel_tile, ((1,), (1,)))

    return lax.fori_loop(0, right_side.shape[1] // block_cols, advance, acc)


def on_device(points, w_in, w_mid, w_out, lengthscale, probes):
    hidden_one = jax.nn.relu(dot_f32(points, w_in, ((1,), (0,)))).astype(jnp.bfloat16)
    hidden_two = jax.nn.relu(dot_f32(hidden_one, w_mid, ((1,), (0,)))).astype(jnp.bfloat16)
    features = dot_f32(w_out, hidden_two, ((0,), (1,)))
    scaled = (features / lengthscale[:, None]).astype(jnp.bfloat16)
    col_peers = lax.axis_size("col")
    row_peers = lax.axis_size("row")
    local = scaled.shape[1]
    feat_dim = scaled.shape[0]
    probe_rows = probes.shape[0]
    side = augmented(scaled)
    side_rows = side.shape[0]
    joined = jnp.concatenate([side, probes], axis=0)
    block = gather_peers(joined, "col", col_peers)
    left_side = block[:side_rows]
    halves = col_peers // row_peers
    span = block.shape[1] // halves
    col = lax.axis_index("col")
    mine = lax.dynamic_slice_in_dim(block, (col % halves) * span, span, 1)
    pairs = []
    for r in range(row_peers):
        for c in range(col_peers):
            target = (r - c // halves) % row_peers
            pairs.append((r * col_peers + c, target * col_peers + c))
    chunks = 2
    width = span // chunks
    arrived = [
        lax.ppermute(mine[:, k * width:(k + 1) * width], ("row", "col"), pairs)
        for k in range(chunks)
    ]
    acc = jnp.zeros((probe_rows, block.shape[1]), jnp.float32)
    for piece in arrived:
        right_side = column_side(piece[:side_rows], feat_dim)
        acc = fold_columns(left_side, right_side, piece[side_rows:], acc, 256)
    parts = jnp.transpose(acc.reshape(probe_rows, col_peers, local), (1, 0, 2))
    summed = lax.all_to_all(parts, "col", 0, 0, tiled=False)
    return jnp.sum(summed, axis=0)


def solution(mesh):
    in_specs = (P(("row", "col"), None), P(), P(), P(), P(), P(None, ("row", "col")))
    out_specs = P(None, ("row", "col"))
    return jax.shard_map(
        on_device, mesh=mesh, in_specs=in_specs, out_specs=out_specs, check_vma=False
    )
```

```python
import jax
import jax.numpy as jnp
from jax import lax
from jax.sharding import PartitionSpec as P


def dot_f32(left, right, dims):
    return lax.dot_general(
        left, right, (dims, ((), ())), preferred_element_type=jnp.float32
    )


def matern_tile(left_feats, left_sq, right_doubled, right_sq):
    cross_term = dot_f32(left_feats, right_doubled, ((0,), (0,)))
    dist_sq = jnp.maximum(left_sq[:, None] + right_sq[None, :] + cross_term, 0.0)
    scaled_dist = jnp.sqrt(5.0 * dist_sq)
    values = (1.0 + scaled_dist + scaled_dist * scaled_dist / 3.0) * jnp.exp(-scaled_dist)
    return values.astype(jnp.bfloat16)


def gather_peers(block, axis, peers):
    spread = jnp.broadcast_to(block[None], (peers,) + block.shape)
    arrived = lax.all_to_all(spread, axis, 0, 0, tiled=False)
    rows = block.shape[0]
    return jnp.transpose(arrived, (1, 0, 2)).reshape(rows, peers * block.shape[1])


def fold_columns(row_feats, row_sq, feats, probes, acc, block_cols):
    wide = feats.astype(jnp.float32)
    sq_norm = jnp.sum(wide * wide, axis=0)
    doubled = (wide * -2.0).astype(jnp.bfloat16)

    def advance(position, row_acc):
        column_start = position * block_cols
        feats_block = lax.dynamic_slice_in_dim(doubled, column_start, block_cols, 1)
        sq_block = lax.dynamic_slice_in_dim(sq_norm, column_start, block_cols, 0)
        probes_block = lax.dynamic_slice_in_dim(probes, column_start, block_cols, 1)
        kernel_tile = matern_tile(row_feats, row_sq, feats_block, sq_block)
        return row_acc + dot_f32(probes_block, kernel_tile, ((1,), (1,)))

    return lax.fori_loop(0, feats.shape[1] // block_cols, advance, acc)


def on_device(points, w_in, w_mid, w_out, lengthscale, probes):
    hidden_one = jax.nn.relu(dot_f32(points, w_in, ((1,), (0,)))).astype(jnp.bfloat16)
    hidden_two = jax.nn.relu(dot_f32(hidden_one, w_mid, ((1,), (0,)))).astype(jnp.bfloat16)
    features = dot_f32(w_out, hidden_two, ((0,), (1,)))
    scaled = (features / lengthscale[:, None]).astype(jnp.bfloat16)
    col_peers = lax.axis_size("col")
    row_peers = lax.axis_size("row")
    local = scaled.shape[1]
    feat_dim = scaled.shape[0]
    probe_rows = probes.shape[0]
    joined = jnp.concatenate([scaled, probes], axis=0)
    block = gather_peers(joined, "col", col_peers)
    row_feats = block[:feat_dim]
    row_wide = row_feats.astype(jnp.float32)
    row_sq = jnp.sum(row_wide * row_wide, axis=0)
    halves = col_peers // row_peers
    span = block.shape[1] // halves
    col = lax.axis_index("col")
    mine = lax.dynamic_slice_in_dim(block, (col % halves) * span, span, 1)
    pairs = []
    for r in range(row_peers):
        for c in range(col_peers):
            target = (r - c // halves) % row_peers
            pairs.append((r * col_peers + c, target * col_peers + c))
    chunks = 2
    width = span // chunks
    arrived = [
        lax.ppermute(mine[:, k * width:(k + 1) * width], ("row", "col"), pairs)
        for k in range(chunks)
    ]
    acc = jnp.zeros((probe_rows, block.shape[1]), jnp.float32)
    for piece in arrived:
        acc = fold_columns(row_feats, row_sq, piece[:feat_dim], piece[feat_dim:], acc, 640)
    parts = jnp.transpose(acc.reshape(probe_rows, col_peers, local), (1, 0, 2))
    summed = lax.all_to_all(parts, "col", 0, 0, tiled=False)
    return jnp.sum(summed, axis=0)


def solution(mesh):
    in_specs = (P(("row", "col"), None), P(), P(), P(), P(), P(None, ("row", "col")))
    out_specs = P(None, ("row", "col"))
    return jax.shard_map(
        on_device, mesh=mesh, in_specs=in_specs, out_specs=out_specs, check_vma=False
    )
```

```python
import jax
import jax.numpy as jnp
from jax import lax
from jax.sharding import PartitionSpec as P


def dot_f32(left, right, dims):
    return lax.dot_general(
        left, right, (dims, ((), ())), preferred_element_type=jnp.float32
    )


def matern_tile(left_feats, left_sq, right_doubled, right_sq):
    cross_term = dot_f32(left_feats, right_doubled, ((0,), (0,)))
    dist_sq = jnp.maximum(left_sq[:, None] + right_sq[None, :] + cross_term, 0.0)
    scaled_dist = jnp.sqrt(5.0 * dist_sq)
    values = (1.0 + scaled_dist + scaled_dist * scaled_dist / 3.0) * jnp.exp(-scaled_dist)
    return values.astype(jnp.bfloat16)


def gather_peers(block, axis, peers):
    spread = jnp.broadcast_to(block[None], (peers,) + block.shape)
    arrived = lax.all_to_all(spread, axis, 0, 0, tiled=False)
    rows = block.shape[0]
    return jnp.transpose(arrived, (1, 0, 2)).reshape(rows, peers * block.shape[1])


def fold_columns(row_feats, row_sq, feats, probes, acc, block_cols):
    wide = feats.astype(jnp.float32)
    sq_norm = jnp.sum(wide * wide, axis=0)
    doubled = (wide * -2.0).astype(jnp.bfloat16)

    def advance(position, row_acc):
        column_start = position * block_cols
        feats_block = lax.dynamic_slice_in_dim(doubled, column_start, block_cols, 1)
        sq_block = lax.dynamic_slice_in_dim(sq_norm, column_start, block_cols, 0)
        probes_block = lax.dynamic_slice_in_dim(probes, column_start, block_cols, 1)
        kernel_tile = matern_tile(row_feats, row_sq, feats_block, sq_block)
        return row_acc + dot_f32(probes_block, kernel_tile, ((1,), (1,)))

    return lax.fori_loop(0, feats.shape[1] // block_cols, advance, acc)


def on_device(points, w_in, w_mid, w_out, lengthscale, probes):
    hidden_one = jax.nn.relu(dot_f32(points, w_in, ((1,), (0,)))).astype(jnp.bfloat16)
    hidden_two = jax.nn.relu(dot_f32(hidden_one, w_mid, ((1,), (0,)))).astype(jnp.bfloat16)
    features = dot_f32(w_out, hidden_two, ((0,), (1,)))
    scaled = (features / lengthscale[:, None]).astype(jnp.bfloat16)
    col_peers = lax.axis_size("col")
    row_peers = lax.axis_size("row")
    local = scaled.shape[1]
    feat_dim = scaled.shape[0]
    probe_rows = probes.shape[0]
    joined = jnp.concatenate([scaled, probes], axis=0)
    block = gather_peers(joined, "col", col_peers)
    row_feats = block[:feat_dim]
    row_wide = row_feats.astype(jnp.float32)
    row_sq = jnp.sum(row_wide * row_wide, axis=0)
    halves = col_peers // row_peers
    span = block.shape[1] // halves
    col = lax.axis_index("col")
    mine = lax.dynamic_slice_in_dim(block, (col % halves) * span, span, 1)
    pairs = []
    for r in range(row_peers):
        for c in range(col_peers):
            target = (r - c // halves) % row_peers
            pairs.append((r * col_peers + c, target * col_peers + c))
    chunks = 1
    width = span // chunks
    arrived = [
        lax.ppermute(mine[:, k * width:(k + 1) * width], ("row", "col"), pairs)
        for k in range(chunks)
    ]
    acc = jnp.zeros((probe_rows, block.shape[1]), jnp.float32)
    for piece in arrived:
        acc = fold_columns(row_feats, row_sq, piece[:feat_dim], piece[feat_dim:], acc, 640)
    parts = jnp.transpose(acc.reshape(probe_rows, col_peers, local), (1, 0, 2))
    summed = lax.all_to_all(parts, "col", 0, 0, tiled=False)
    return jnp.sum(summed, axis=0)


def solution(mesh):
    in_specs = (P(("row", "col"), None), P(), P(), P(), P(), P(None, ("row", "col")))
    out_specs = P(None, ("row", "col"))
    return jax.shard_map(
        on_device, mesh=mesh, in_specs=in_specs, out_specs=out_specs, check_vma=False
    )
```

```python
import jax
import jax.numpy as jnp
from jax import lax
from jax.sharding import PartitionSpec as P


def dot_f32(left, right, dims):
    return lax.dot_general(
        left, right, (dims, ((), ())), preferred_element_type=jnp.float32
    )


def matern_tile(left_feats, left_sq, right_doubled, right_sq):
    cross_term = dot_f32(left_feats, right_doubled, ((0,), (0,)))
    dist_sq = jnp.maximum(left_sq[:, None] + right_sq[None, :] + cross_term, 0.0)
    scaled_dist = jnp.sqrt(5.0 * dist_sq)
    values = (1.0 + scaled_dist + scaled_dist * scaled_dist / 3.0) * jnp.exp(-scaled_dist)
    return values.astype(jnp.bfloat16)


def gather_peers(block, axis, peers):
    spread = jnp.broadcast_to(block[None], (peers,) + block.shape)
    arrived = lax.all_to_all(spread, axis, 0, 0, tiled=False)
    rows = block.shape[0]
    return jnp.transpose(arrived, (1, 0, 2)).reshape(rows, peers * block.shape[1])


def fold_columns(row_feats, row_sq, feats, probes, acc, block_cols):
    wide = feats.astype(jnp.float32)
    sq_norm = jnp.sum(wide * wide, axis=0)
    doubled = (wide * -2.0).astype(jnp.bfloat16)

    def advance(position, row_acc):
        column_start = position * block_cols
        feats_block = lax.dynamic_slice_in_dim(doubled, column_start, block_cols, 1)
        sq_block = lax.dynamic_slice_in_dim(sq_norm, column_start, block_cols, 0)
        probes_block = lax.dynamic_slice_in_dim(probes, column_start, block_cols, 1)
        kernel_tile = matern_tile(row_feats, row_sq, feats_block, sq_block)
        return row_acc + dot_f32(probes_block, kernel_tile, ((1,), (1,)))

    return lax.fori_loop(0, feats.shape[1] // block_cols, advance, acc)


def on_device(points, w_in, w_mid, w_out, lengthscale, probes):
    hidden_one = jax.nn.relu(dot_f32(points, w_in, ((1,), (0,)))).astype(jnp.bfloat16)
    hidden_two = jax.nn.relu(dot_f32(hidden_one, w_mid, ((1,), (0,)))).astype(jnp.bfloat16)
    features = dot_f32(w_out, hidden_two, ((0,), (1,)))
    scaled = (features / lengthscale[:, None]).astype(jnp.bfloat16)
    col_peers = lax.axis_size("col")
    row_peers = lax.axis_size("row")
    local = scaled.shape[1]
    feat_dim = scaled.shape[0]
    probe_rows = probes.shape[0]
    joined = jnp.concatenate([scaled, probes], axis=0)
    block = gather_peers(joined, "col", col_peers)
    row_feats = block[:feat_dim]
    row_wide = row_feats.astype(jnp.float32)
    row_sq = jnp.sum(row_wide * row_wide, axis=0)
    halves = col_peers // row_peers
    span = block.shape[1] // halves
    col = lax.axis_index("col")
    mine = lax.dynamic_slice_in_dim(block, (col % halves) * span, span, 1)
    pairs = []
    for r in range(row_peers):
        for c in range(col_peers):
            target = (r - c // halves) % row_peers
            pairs.append((r * col_peers + c, target * col_peers + c))
    chunks = 2
    width = span // chunks
    arrived = [
        lax.ppermute(mine[:, k * width:(k + 1) * width], ("row", "col"), pairs)
        for k in range(chunks)
    ]
    row_halves = 2
    part = local // row_halves
    feats_split = row_feats.reshape(feat_dim, col_peers, row_halves, part)
    sq_split = row_sq.reshape(col_peers, row_halves, part)
    results = []
    for h in range(row_halves):
        half_feats = feats_split[:, :, h, :].reshape(feat_dim, col_peers * part)
        half_sq = sq_split[:, h, :].reshape(col_peers * part)
        acc = jnp.zeros((probe_rows, col_peers * part), jnp.float32)
        for piece in arrived:
            acc = fold_columns(half_feats, half_sq, piece[:feat_dim], piece[feat_dim:], acc, 640)
        parts = jnp.transpose(acc.reshape(probe_rows, col_peers, part), (1, 0, 2))
        summed = lax.all_to_all(parts, "col", 0, 0, tiled=False)
        results.append(jnp.sum(summed, axis=0))
    return jnp.concatenate(results, axis=1)


def solution(mesh):
    in_specs = (P(("row", "col"), None), P(), P(), P(), P(), P(None, ("row", "col")))
    out_specs = P(None, ("row", "col"))
    return jax.shard_map(
        on_device, mesh=mesh, in_specs=in_specs, out_specs=out_specs, check_vma=False
    )
```

```python
import jax
import jax.numpy as jnp
from jax import lax
from jax.sharding import PartitionSpec as P


def dot_f32(left, right, dims):
    return lax.dot_general(
        left, right, (dims, ((), ())), preferred_element_type=jnp.float32
    )


def matern_tile(left_feats, left_sq, right_doubled, right_sq):
    cross_term = dot_f32(right_doubled, left_feats, ((0,), (0,)))
    dist_sq = jnp.maximum(left_sq[None, :] + right_sq[:, None] + cross_term, 0.0)
    scaled_dist = jnp.sqrt(5.0 * dist_sq)
    values = (1.0 + scaled_dist + scaled_dist * scaled_dist / 3.0) * jnp.exp(-scaled_dist)
    return values.astype(jnp.bfloat16)


def gather_peers(block, axis, peers):
    spread = jnp.broadcast_to(block[None], (peers,) + block.shape)
    arrived = lax.all_to_all(spread, axis, 0, 0, tiled=False)
    rows = block.shape[0]
    return jnp.transpose(arrived, (1, 0, 2)).reshape(rows, peers * block.shape[1])


def fold_columns(row_feats, row_sq, feats, probes, acc, block_cols):
    wide = feats.astype(jnp.float32)
    sq_norm = jnp.sum(wide * wide, axis=0)
    doubled = (wide * -2.0).astype(jnp.bfloat16)

    def advance(position, row_acc):
        column_start = position * block_cols
        feats_block = lax.dynamic_slice_in_dim(doubled, column_start, block_cols, 1)
        sq_block = lax.dynamic_slice_in_dim(sq_norm, column_start, block_cols, 0)
        probes_block = lax.dynamic_slice_in_dim(probes, column_start, block_cols, 1)
        kernel_tile = matern_tile(row_feats, row_sq, feats_block, sq_block)
        return row_acc + dot_f32(probes_block, kernel_tile, ((1,), (0,)))

    return lax.fori_loop(0, feats.shape[1] // block_cols, advance, acc)


def on_device(points, w_in, w_mid, w_out, lengthscale, probes):
    hidden_one = jax.nn.relu(dot_f32(points, w_in, ((1,), (0,)))).astype(jnp.bfloat16)
    hidden_two = jax.nn.relu(dot_f32(hidden_one, w_mid, ((1,), (0,)))).astype(jnp.bfloat16)
    features = dot_f32(w_out, hidden_two, ((0,), (1,)))
    scaled = (features / lengthscale[:, None]).astype(jnp.bfloat16)
    col_peers = lax.axis_size("col")
    row_peers = lax.axis_size("row")
    local = scaled.shape[1]
    feat_dim = scaled.shape[0]
    probe_rows = probes.shape[0]
    joined = jnp.concatenate([scaled, probes], axis=0)
    block = gather_peers(joined, "col", col_peers)
    row_feats = block[:feat_dim]
    row_wide = row_feats.astype(jnp.float32)
    row_sq = jnp.sum(row_wide * row_wide, axis=0)
    halves = col_peers // row_peers
    span = block.shape[1] // halves
    col = lax.axis_index("col")
    mine = lax.dynamic_slice_in_dim(block, (col % halves) * span, span, 1)
    pairs = []
    for r in range(row_peers):
        for c in range(col_peers):
            target = (r - c // halves) % row_peers
            pairs.append((r * col_peers + c, target * col_peers + c))
    chunks = 2
    width = span // chunks
    arrived = [
        lax.ppermute(mine[:, k * width:(k + 1) * width], ("row", "col"), pairs)
        for k in range(chunks)
    ]
    acc = jnp.zeros((probe_rows, block.shape[1]), jnp.float32)
    for piece in arrived:
        acc = fold_columns(row_feats, row_sq, piece[:feat_dim], piece[feat_dim:], acc, 640)
    parts = jnp.transpose(acc.reshape(probe_rows, col_peers, local), (1, 0, 2))
    summed = lax.all_to_all(parts, "col", 0, 0, tiled=False)
    return jnp.sum(summed, axis=0)


def solution(mesh):
    in_specs = (P(("row", "col"), None), P(), P(), P(), P(), P(None, ("row", "col")))
    out_specs = P(None, ("row", "col"))
    return jax.shard_map(
        on_device, mesh=mesh, in_specs=in_specs, out_specs=out_specs, check_vma=False
    )
```

```python
import jax
import jax.numpy as jnp
from jax import lax
from jax.sharding import PartitionSpec as P


def dot_f32(left, right, dims):
    return lax.dot_general(
        left, right, (dims, ((), ())), preferred_element_type=jnp.float32
    )


def matern_tile(left_feats, left_sq, right_doubled, right_sq):
    cross_term = dot_f32(left_feats, right_doubled, ((0,), (0,)))
    dist_sq = jnp.maximum(left_sq[:, None] + right_sq[None, :] + cross_term, 0.0)
    scaled_dist = jnp.sqrt(5.0 * dist_sq)
    values = (1.0 + scaled_dist + scaled_dist * scaled_dist / 3.0) * jnp.exp(-scaled_dist)
    return values.astype(jnp.bfloat16)


def gather_peers(block, axis, peers):
    spread = jnp.broadcast_to(block[None], (peers,) + block.shape)
    arrived = lax.all_to_all(spread, axis, 0, 0, tiled=False)
    rows = block.shape[0]
    return jnp.transpose(arrived, (1, 0, 2)).reshape(rows, peers * block.shape[1])


def fold_columns(row_feats, row_sq, feats, probes, acc, block_cols):
    wide = feats.astype(jnp.float32)
    sq_norm = jnp.sum(wide * wide, axis=0)
    doubled = (wide * -2.0).astype(jnp.bfloat16)

    def advance(position, row_acc):
        column_start = position * block_cols
        feats_block = lax.dynamic_slice_in_dim(doubled, column_start, block_cols, 1)
        sq_block = lax.dynamic_slice_in_dim(sq_norm, column_start, block_cols, 0)
        probes_block = lax.dynamic_slice_in_dim(probes, column_start, block_cols, 1)
        kernel_tile = matern_tile(row_feats, row_sq, feats_block, sq_block)
        return row_acc + dot_f32(probes_block, kernel_tile, ((1,), (1,)))

    return lax.fori_loop(0, feats.shape[1] // block_cols, advance, acc)


def on_device(points, w_in, w_mid, w_out, lengthscale, probes):
    hidden_one = jax.nn.relu(dot_f32(points, w_in, ((1,), (0,)))).astype(jnp.bfloat16)
    hidden_two = jax.nn.relu(dot_f32(hidden_one, w_mid, ((1,), (0,)))).astype(jnp.bfloat16)
    features = dot_f32(w_out, hidden_two, ((0,), (1,)))
    scaled = (features / lengthscale[:, None]).astype(jnp.bfloat16)
    col_peers = lax.axis_size("col")
    row_peers = lax.axis_size("row")
    local = scaled.shape[1]
    feat_dim = scaled.shape[0]
    probe_rows = probes.shape[0]
    joined = jnp.concatenate([scaled, probes], axis=0)
    block = gather_peers(joined, "col", col_peers)
    row_feats = block[:feat_dim]
    row_wide = row_feats.astype(jnp.float32)
    row_sq = jnp.sum(row_wide * row_wide, axis=0)
    halves = col_peers // row_peers
    span = block.shape[1] // halves
    col = lax.axis_index("col")
    mine = lax.dynamic_slice_in_dim(block, (col % halves) * span, span, 1)
    z_run = 4
    swap = [0, 3, 2, 1]
    pairs = []
    for r in range(row_peers):
        for c in range(col_peers):
            chip, core = divmod(c, halves)
            source_chip = (chip // z_run) * z_run + swap[chip % z_run]
            source = ((r + chip) % row_peers) * col_peers + source_chip * halves + core
            pairs.append((source, r * col_peers + c))
    chunks = 2
    width = span // chunks
    arrived = [
        lax.ppermute(mine[:, k * width:(k + 1) * width], ("row", "col"), pairs)
        for k in range(chunks)
    ]
    acc = jnp.zeros((probe_rows, block.shape[1]), jnp.float32)
    for piece in arrived:
        acc = fold_columns(row_feats, row_sq, piece[:feat_dim], piece[feat_dim:], acc, 640)
    parts = jnp.transpose(acc.reshape(probe_rows, col_peers, local), (1, 0, 2))
    summed = lax.all_to_all(parts, "col", 0, 0, tiled=False)
    return jnp.sum(summed, axis=0)


def solution(mesh):
    in_specs = (P(("row", "col"), None), P(), P(), P(), P(), P(None, ("row", "col")))
    out_specs = P(None, ("row", "col"))
    return jax.shard_map(
        on_device, mesh=mesh, in_specs=in_specs, out_specs=out_specs, check_vma=False
    )
```

```python
import jax
import jax.numpy as jnp
from jax import lax
from jax.sharding import PartitionSpec as P


def dot_f32(left, right, dims):
    return lax.dot_general(
        left, right, (dims, ((), ())), preferred_element_type=jnp.float32
    )


def matern_tile(left_feats, left_sq, right_doubled, right_sq):
    cross_term = dot_f32(left_feats, right_doubled, ((0,), (0,)))
    dist_sq = jnp.maximum(left_sq[:, None] + right_sq[None, :] + cross_term, 0.0)
    scaled_dist = jnp.sqrt(5.0 * dist_sq)
    values = (1.0 + scaled_dist + scaled_dist * scaled_dist / 3.0) * jnp.exp(-scaled_dist)
    return values.astype(jnp.bfloat16)


def gather_peers(block, axis, peers):
    spread = jnp.broadcast_to(block[None], (peers,) + block.shape)
    arrived = lax.all_to_all(spread, axis, 0, 0, tiled=False)
    rows = block.shape[0]
    return jnp.transpose(arrived, (1, 0, 2)).reshape(rows, peers * block.shape[1])


def fold_columns(row_feats, row_sq, feats, probes, acc, block_cols):
    wide = feats.astype(jnp.float32)
    sq_norm = jnp.sum(wide * wide, axis=0)
    doubled = (wide * -2.0).astype(jnp.bfloat16)

    def advance(position, row_acc):
        column_start = position * block_cols
        feats_block = lax.dynamic_slice_in_dim(doubled, column_start, block_cols, 1)
        sq_block = lax.dynamic_slice_in_dim(sq_norm, column_start, block_cols, 0)
        probes_block = lax.dynamic_slice_in_dim(probes, column_start, block_cols, 1)
        kernel_tile = matern_tile(row_feats, row_sq, feats_block, sq_block)
        return row_acc + dot_f32(probes_block, kernel_tile, ((1,), (1,)))

    return lax.fori_loop(0, feats.shape[1] // block_cols, advance, acc)


def on_device(points, w_in, w_mid, w_out, lengthscale, probes):
    hidden_one = jax.nn.relu(dot_f32(points, w_in, ((1,), (0,)))).astype(jnp.bfloat16)
    hidden_two = jax.nn.relu(dot_f32(hidden_one, w_mid, ((1,), (0,)))).astype(jnp.bfloat16)
    features = dot_f32(w_out, hidden_two, ((0,), (1,)))
    scaled = (features / lengthscale[:, None]).astype(jnp.bfloat16)
    col_peers = lax.axis_size("col")
    row_peers = lax.axis_size("row")
    local = scaled.shape[1]
    feat_dim = scaled.shape[0]
    probe_rows = probes.shape[0]
    joined = jnp.concatenate([scaled, probes], axis=0)
    block = gather_peers(joined, "col", col_peers)
    row_feats = block[:feat_dim]
    row_wide = row_feats.astype(jnp.float32)
    row_sq = jnp.sum(row_wide * row_wide, axis=0)
    halves = col_peers // row_peers
    span = block.shape[1] // halves
    col = lax.axis_index("col")
    z_run = 4
    swap = [0, 3, 2, 1]
    chunks = halves
    width = span // chunks
    arrived = []
    for k in range(chunks):
        pairs = []
        for r in range(row_peers):
            for c in range(col_peers):
                chip, core = divmod(c, halves)
                source_chip = (chip // z_run) * z_run + swap[chip % z_run]
                sender = source_chip * halves + (core + k) % halves
                source = ((r + chip) % row_peers) * col_peers + sender
                pairs.append((source, r * col_peers + c))
        wanted = (col % halves + halves - k) % halves
        mine = lax.dynamic_slice_in_dim(block, wanted * span + k * width, width, 1)
        arrived.append(lax.ppermute(mine, ("row", "col"), pairs))
    acc = jnp.zeros((probe_rows, block.shape[1]), jnp.float32)
    for piece in arrived:
        acc = fold_columns(row_feats, row_sq, piece[:feat_dim], piece[feat_dim:], acc, 640)
    parts = jnp.transpose(acc.reshape(probe_rows, col_peers, local), (1, 0, 2))
    summed = lax.all_to_all(parts, "col", 0, 0, tiled=False)
    return jnp.sum(summed, axis=0)


def solution(mesh):
    in_specs = (P(("row", "col"), None), P(), P(), P(), P(), P(None, ("row", "col")))
    out_specs = P(None, ("row", "col"))
    return jax.shard_map(
        on_device, mesh=mesh, in_specs=in_specs, out_specs=out_specs, check_vma=False
    )
```

```python
import jax
import jax.numpy as jnp
from jax import lax
from jax.sharding import PartitionSpec as P


def dot_f32(left, right, dims):
    return lax.dot_general(
        left, right, (dims, ((), ())), preferred_element_type=jnp.float32
    )


def matern_tile(left_feats, left_sq, right_doubled, right_sq):
    cross_term = dot_f32(left_feats, right_doubled, ((0,), (0,)))
    dist_sq = jnp.maximum(left_sq[:, None] + right_sq[None, :] + cross_term, 0.0)
    scaled_dist = jnp.sqrt(5.0 * dist_sq)
    values = (1.0 + scaled_dist + scaled_dist * scaled_dist / 3.0) * jnp.exp(-scaled_dist)
    return values.astype(jnp.bfloat16)


def gather_peers(block, axis, peers):
    spread = jnp.broadcast_to(block[None], (peers,) + block.shape)
    arrived = lax.all_to_all(spread, axis, 0, 0, tiled=False)
    rows = block.shape[0]
    return jnp.transpose(arrived, (1, 0, 2)).reshape(rows, peers * block.shape[1])


def fold_columns(row_feats, row_sq, feats, probes, acc, block_cols):
    wide = feats.astype(jnp.float32)
    sq_norm = jnp.sum(wide * wide, axis=0)
    doubled = (wide * -2.0).astype(jnp.bfloat16)

    def advance(position, row_acc):
        column_start = position * block_cols
        feats_block = lax.dynamic_slice_in_dim(doubled, column_start, block_cols, 1)
        sq_block = lax.dynamic_slice_in_dim(sq_norm, column_start, block_cols, 0)
        probes_block = lax.dynamic_slice_in_dim(probes, column_start, block_cols, 1)
        kernel_tile = matern_tile(row_feats, row_sq, feats_block, sq_block)
        return row_acc + dot_f32(probes_block, kernel_tile, ((1,), (1,)))

    return lax.fori_loop(0, feats.shape[1] // block_cols, advance, acc)


def on_device(points, w_in, w_mid, w_out, lengthscale, probes):
    hidden_one = jax.nn.relu(dot_f32(points, w_in, ((1,), (0,)))).astype(jnp.bfloat16)
    hidden_two = jax.nn.relu(dot_f32(hidden_one, w_mid, ((1,), (0,)))).astype(jnp.bfloat16)
    features = dot_f32(w_out, hidden_two, ((0,), (1,)))
    scaled = (features / lengthscale[:, None]).astype(jnp.bfloat16)
    col_peers = lax.axis_size("col")
    row_peers = lax.axis_size("row")
    local = scaled.shape[1]
    feat_dim = scaled.shape[0]
    probe_rows = probes.shape[0]
    joined = jnp.concatenate([scaled, probes], axis=0)
    block = gather_peers(joined, "col", col_peers)
    row_feats = block[:feat_dim]
    row_wide = row_feats.astype(jnp.float32)
    row_sq = jnp.sum(row_wide * row_wide, axis=0)
    halves = col_peers // row_peers
    span = block.shape[1] // halves
    col = lax.axis_index("col")
    z_run = 4
    swap = [0, 3, 2, 1]
    swaps = [swap, [1, 2, 3, 0]]
    chunks = 2 * halves
    width = span // chunks
    arrived = []
    for k in range(chunks):
        pairs = []
        for r in range(row_peers):
            for c in range(col_peers):
                chip, core = divmod(c, halves)
                source_chip = (chip // z_run) * z_run + swaps[k // halves][chip % z_run]
                sender = source_chip * halves + (core + k) % halves
                source = ((r + chip) % row_peers) * col_peers + sender
                pairs.append((source, r * col_peers + c))
        wanted = (col % halves + halves - k) % halves
        mine = lax.dynamic_slice_in_dim(block, wanted * span + k * width, width, 1)
        arrived.append(lax.ppermute(mine, ("row", "col"), pairs))
    acc = jnp.zeros((probe_rows, block.shape[1]), jnp.float32)
    for piece in arrived:
        acc = fold_columns(row_feats, row_sq, piece[:feat_dim], piece[feat_dim:], acc, 320)
    parts = jnp.transpose(acc.reshape(probe_rows, col_peers, local), (1, 0, 2))
    summed = lax.all_to_all(parts, "col", 0, 0, tiled=False)
    return jnp.sum(summed, axis=0)


def solution(mesh):
    in_specs = (P(("row", "col"), None), P(), P(), P(), P(), P(None, ("row", "col")))
    out_specs = P(None, ("row", "col"))
    return jax.shard_map(
        on_device, mesh=mesh, in_specs=in_specs, out_specs=out_specs, check_vma=False
    )
```
